512 devices in a mesh: docs: 128 (over y, z, core), grp: 4 (over x).
Axes of the slice: x: 4, y: 8, z: 8, core: 2. Of those that a mesh axis runs over, the one named last changes fastest.
Arguments:
- embeddings: bfloat16 [131072, 1024], P(('docs', 'grp')), may hold values from -6 to 6
- projection: bfloat16 [1024, 512], replicated, may hold values from -0.1875 to 0.1875
- phase_code: int32 [1], replicated, may hold values from 0 to 1023
- penalty: int32 [1], replicated, may hold values from 1 to 16
- assignment: int32 [512, 256], P(('docs', 'grp')), may hold values from 0 to 255, each once within a row
- targets: bfloat16 [131072, 256], P(('docs', 'grp')), may hold values from -7 to 7
Outputs:
- quality: bfloat16 [131072, 256], P(('docs', 'grp'))
The draws below stay inside these ranges and needn't reach their ends.
Inputs may be any that keep to these rules, and one draw needn't show every extreme that they name: Each row of assignment names every row of its slab once.
All inputs are finite; a program needn't handle non-finite values. Where the reference program divides by a largest or mean magnitude, that divisor is 1e-20 or more.
Results may differ from the reference program's by a relative error of at most 0.0056.
Values sent between devices are 32-bit elements; how exact they have to be, the bound alone decides.
No kernel may reach another device: no remote copies, remote signals or barrier semaphores. Data moves between devices by JAX's collectives and lax.ppermute only.
A program may use at most 64 MiB of HBM per device.

```python
import math
import jax
import jax.numpy as jnp
from jax import lax

EMB = 1024
FEAT = 512
ATTR = 256
ROWS_DEV = 256
SLABS = 512
TOTAL = 131072


def draw_targets(key, part):
    offsets = jax.random.uniform(jax.random.fold_in(key, 7), (ATTR,), jnp.float32, -1.5, 1.5)
    noise = jnp.clip(jax.random.normal(key, (TOTAL, ATTR), jnp.float32), -5.0, 5.0)
    return (noise + offsets).astype(jnp.bfloat16)


def level_of(key, extent, shards, smallest, top_value):
    factor_of = 1.0
    for dim, parts in shards:
        steps = jax.random.uniform(jax.random.fold_in(jax.random.fold_in(key, 6), dim), (parts,), jnp.float32, smallest / len(shards), top_value / len(shards))
        factor_of = factor_of * jnp.repeat(jnp.exp(steps), extent[dim] // parts).reshape((-1,) + (1,) * (len(extent) - 1 - dim))
    return factor_of


def normal_values(rng, dims, width, bound, pieces=(), held_as=jnp.bfloat16):
    factor_of = level_of(rng, dims, pieces, -0.22, 0.18) if pieces else 1.0
    entries = jax.random.normal(rng, dims, jnp.float32) * width * factor_of
    return jnp.minimum(jnp.maximum(entries, -bound), bound).astype(held_as)


def setup_inputs(seed: int = 0) -> dict:
    streams_of = jax.random.split(jax.random.key(seed), 7)
    return {
        "embeddings": normal_values(streams_of[0], (TOTAL, EMB), 1.0, 6.0, ((0, 512),)),
        "projection": normal_values(streams_of[1], (EMB, FEAT), EMB ** -0.5, 0.1875),
        "phase_code": jax.random.randint(streams_of[2], (1,), 0, 1024).astype(jnp.int32),
        "penalty": jax.random.randint(streams_of[3], (1,), 1, 17).astype(jnp.int32),
        "assignment": jax.vmap(lambda own: jax.random.permutation(own, ROWS_DEV))(jax.random.split(streams_of[4], SLABS)).reshape((SLABS, ROWS_DEV)).astype(jnp.int32),
        "targets": draw_targets(jax.random.fold_in(streams_of[6], 71), 0),
    }


def phase_table(phase_code):
    feature_ids = jnp.arange(FEAT, dtype=jnp.int32)
    code_value = phase_code[0].astype(jnp.int32)
    index_value = (code_value * 389 + feature_ids * (feature_ids + code_value) * 53) % 4096
    return index_value.astype(jnp.float32) * (2.0 * math.pi / 4096.0)

def featurize(block, projection, phases):
    projected = jnp.dot(block.astype(jnp.float32), projection.astype(jnp.float32), preferred_element_type=jnp.float32)
    return jnp.cos(projected + phases).astype(jnp.bfloat16)

def reference(embeddings, projection, phase_code, penalty, assignment, targets):
    phases = phase_table(phase_code)
    slab_emb = embeddings.reshape(SLABS, ROWS_DEV, EMB)
    slab_tgt = targets.reshape(SLABS, ROWS_DEV, ATTR)

    def accumulate(carry, inputs):
        block, order, labels = inputs
        features = featurize(block, projection, phases)
        aligned = features[order.astype(jnp.int32)]
        gram = carry[0] + jnp.dot(features.T.astype(jnp.float32), features.astype(jnp.float32), preferred_element_type=jnp.float32)
        cross = carry[1] + jnp.dot(aligned.T.astype(jnp.float32), labels.astype(jnp.float32), preferred_element_type=jnp.float32)
        return ((gram, cross), None)
    start = (jnp.zeros((FEAT, FEAT), jnp.float32), jnp.zeros((FEAT, ATTR), jnp.float32))
    (gram, cross), unused = lax.scan(accumulate, start, (slab_emb, assignment, slab_tgt))
    ridge_shift = penalty[0].astype(jnp.float32) * jnp.float32(TOTAL / 8.0)
    system = gram + ridge_shift * jnp.eye(FEAT, dtype=jnp.float32)
    factor = jnp.linalg.cholesky(system)
    coeffs = jax.scipy.linalg.cho_solve((factor, True), cross).astype(jnp.bfloat16)

    def score_slab(block):
        features = featurize(block, projection, phases)
        return jnp.dot(features.astype(jnp.float32), coeffs.astype(jnp.float32), preferred_element_type=jnp.float32)
    scores = lax.map(score_slab, slab_emb).reshape(TOTAL, ATTR)
    peak = jnp.max(jnp.abs(scores), axis=0)
    total = jnp.sum(scores, axis=0)
    quality = (scores - total / jnp.float32(TOTAL)) / (peak + 1e-06)
    return quality.astype(jnp.bfloat16)
```

```python
import math

import jax
import jax.numpy as jnp
from jax import lax
from jax.sharding import PartitionSpec as P


def phase_table(phase_code, width):
    feature_ids = jnp.arange(width, dtype=jnp.int32)
    code_value = phase_code[0]
    index_value = (code_value * 389 + feature_ids * (feature_ids + code_value) * 53) % 4096
    return index_value.astype(jnp.float32) * (2.0 * math.pi / 4096.0)


def exchange_bits(axis_sizes):
    bits = []
    for name, size in axis_sizes:
        mask = 1
        while mask < size:
            bits.append((name, size, mask))
            mask *= 2
    return bits


def partner(x, name, size, mask):
    return lax.ppermute(x, name, [(i, i ^ mask) for i in range(size)])


def tree_sum(x, bits, halving):
    for name, size, mask in bits[:halving]:
        half = x.shape[0] // 2
        bit = (lax.axis_index(name) // mask) % 2
        keep = lax.dynamic_slice_in_dim(x, bit * half, half, 0)
        send = lax.dynamic_slice_in_dim(x, (1 - bit) * half, half, 0)
        x = keep + partner(send, name, size, mask)
    for name, size, mask in bits[halving:]:
        x = x + partner(x, name, size, mask)
    for name, size, mask in reversed(bits[:halving]):
        bit = (lax.axis_index(name) // mask) % 2
        other = partner(x, name, size, mask)
        x = jnp.where(bit == 0, jnp.concatenate([x, other]), jnp.concatenate([other, x]))
    return x


def peak_and_total(stats, bits):
    for name, size, mask in bits:
        other = partner(stats, name, size, mask)
        stats = jnp.concatenate(
            [jnp.maximum(stats[:1], other[:1]), stats[1:] + other[1:]], axis=0
        )
    return stats


def on_device(embeddings, projection, phase_code, penalty, assignment, targets):
    width = projection.shape[1]
    attrs = targets.shape[1]
    bits = exchange_bits([("docs", lax.axis_size("docs")), ("grp", lax.axis_size("grp"))])
    phases = phase_table(phase_code, width)
    projected = jnp.dot(embeddings, projection, preferred_element_type=jnp.float32)
    features = jnp.cos(projected + phases).astype(jnp.bfloat16)
    aligned = features[assignment.reshape(-1)]
    gram_part = lax.dot_general(
        features, features, (((0,), (0,)), ((), ())), preferred_element_type=jnp.float32
    )
    cross_part = lax.dot_general(
        aligned, targets, (((0,), (0,)), ((), ())), preferred_element_type=jnp.float32
    )
    packed = jnp.concatenate([gram_part, cross_part], axis=1)
    flat = packed.reshape(-1, 128)
    summed = tree_sum(flat, bits, 3).reshape(width, width + attrs)
    gram = summed[:, :width]
    cross = summed[:, width:]
    total_rows = embeddings.shape[0] * lax.axis_size("docs") * lax.axis_size("grp")
    ridge_shift = penalty[0].astype(jnp.float32) * jnp.float32(total_rows / 8.0)
    system = gram + ridge_shift * jnp.eye(width, dtype=jnp.float32)
    factor = jnp.linalg.cholesky(system)
    coeffs = jax.scipy.linalg.cho_solve((factor, True), cross).astype(jnp.bfloat16)
    scores = jnp.dot(features, coeffs, preferred_element_type=jnp.float32)
    peak_local = jnp.max(jnp.abs(scores), axis=0)
    column_sum = jnp.sum(scores, axis=0)
    stats = peak_and_total(jnp.stack([peak_local, column_sum]), bits)
    peak = stats[0]
    total = stats[1]
    quality = (scores - total / jnp.float32(total_rows)) / (peak + 1e-06)
    return quality.astype(jnp.bfloat16)


def solution(mesh):
    in_specs = (
        P(("docs", "grp"), None),
        P(),
        P(),
        P(),
        P(("docs", "grp"), None),
        P(("docs", "grp"), None),
    )
    out_specs = P(("docs", "grp"), None)
    return jax.shard_map(
        on_device, mesh=mesh, in_specs=in_specs, out_specs=out_specs, check_vma=False
    )
```

```python
import math

import jax
import jax.numpy as jnp
from jax import lax
from jax.sharding import PartitionSpec as P


def phase_table(phase_code, width):
    feature_ids = jnp.arange(width, dtype=jnp.int32)
    code_value = phase_code[0]
    index_value = (code_value * 389 + feature_ids * (feature_ids + code_value) * 53) % 4096
    return index_value.astype(jnp.float32) * (2.0 * math.pi / 4096.0)


def exchange_bits(axis_sizes):
    bits = []
    for name, size in axis_sizes:
        mask = 1
        while mask < size:
            bits.append((name, size, mask))
            mask *= 2
    return bits


def partner(x, name, size, mask):
    return lax.ppermute(x, name, [(i, i ^ mask) for i in range(size)])


def tree_sum(x, bits, halving):
    for name, size, mask in bits[:halving]:
        half = x.shape[0] // 2
        bit = (lax.axis_index(name) // mask) % 2
        keep = lax.dynamic_slice_in_dim(x, bit * half, half, 0)
        send = lax.dynamic_slice_in_dim(x, (1 - bit) * half, half, 0)
        x = keep + partner(send, name, size, mask)
    for name, size, mask in bits[halving:]:
        x = x + partner(x, name, size, mask)
    for name, size, mask in reversed(bits[:halving]):
        bit = (lax.axis_index(name) // mask) % 2
        other = partner(x, name, size, mask)
        x = jnp.where(bit == 0, jnp.concatenate([x, other]), jnp.concatenate([other, x]))
    return x


def peak_and_total(stats, bits):
    for name, size, mask in bits:
        other = partner(stats, name, size, mask)
        stats = jnp.concatenate(
            [jnp.maximum(stats[:1], other[:1]), stats[1:] + other[1:]], axis=0
        )
    return stats


def on_device(embeddings, projection, phase_code, penalty, assignment, targets):
    width = projection.shape[1]
    attrs = targets.shape[1]
    bits = exchange_bits([("docs", lax.axis_size("docs")), ("grp", lax.axis_size("grp"))])
    phases = phase_table(phase_code, width)
    projected = jnp.dot(embeddings, projection, preferred_element_type=jnp.float32)
    features = jnp.cos(projected + phases).astype(jnp.bfloat16)
    aligned = features[assignment.reshape(-1)]
    gram_part = lax.dot_general(
        features, features, (((0,), (0,)), ((), ())), preferred_element_type=jnp.float32
    )
    cross_part = lax.dot_general(
        aligned, targets, (((0,), (0,)), ((), ())), preferred_element_type=jnp.float32
    )
    block = 128
    nb = width // block
    lower_blocks = [
        gram_part[i * block:(i + 1) * block, j * block:(j + 1) * block]
        for i in range(nb)
        for j in range(i + 1)
    ]
    gram_flat = jnp.concatenate(lower_blocks, axis=0).reshape(-1, 128)
    gram_sum = tree_sum(gram_flat, bits, 3).reshape(len(lower_blocks), block, block)
    cross = tree_sum(cross_part.reshape(-1, 128), bits, 3).reshape(width, attrs)
    block_of = {}
    for n, (i, j) in enumerate((i, j) for i in range(nb) for j in range(i + 1)):
        block_of[(i, j)] = gram_sum[n]
        block_of[(j, i)] = gram_sum[n].T
    gram = jnp.concatenate(
        [jnp.concatenate([block_of[(i, j)] for j in range(nb)], axis=1) for i in range(nb)],
        axis=0,
    )
    total_rows = embeddings.shape[0] * lax.axis_size("docs") * lax.axis_size("grp")
    ridge_shift = penalty[0].astype(jnp.float32) * jnp.float32(total_rows / 8.0)
    system = gram + ridge_shift * jnp.eye(width, dtype=jnp.float32)
    factor = lax.linalg.cholesky(system, symmetrize_input=False)
    coeffs = jax.scipy.linalg.cho_solve((factor, True), cross).astype(jnp.bfloat16)
    scores = jnp.dot(features, coeffs, preferred_element_type=jnp.float32)
    peak_local = jnp.max(jnp.abs(scores), axis=0)
    column_sum = jnp.sum(scores, axis=0)
    stats = peak_and_total(jnp.stack([peak_local, column_sum]), bits)
    peak = stats[0]
    total = stats[1]
    quality = (scores - total / jnp.float32(total_rows)) / (peak + 1e-06)
    return quality.astype(jnp.bfloat16)


def solution(mesh):
    in_specs = (
        P(("docs", "grp"), None),
        P(),
        P(),
        P(),
        P(("docs", "grp"), None),
        P(("docs", "grp"), None),
    )
    out_specs = P(("docs", "grp"), None)
    return jax.shard_map(
        on_device, mesh=mesh, in_specs=in_specs, out_specs=out_specs, check_vma=False
    )
```

```python
import math

import jax
import jax.numpy as jnp
from jax import lax
from jax.sharding import PartitionSpec as P


def phase_table(phase_code, width):
    feature_ids = jnp.arange(width, dtype=jnp.int32)
    code_value = phase_code[0]
    index_value = (code_value * 389 + feature_ids * (feature_ids + code_value) * 53) % 4096
    return index_value.astype(jnp.float32) * (2.0 * math.pi / 4096.0)


def exchange_bits(axis_sizes):
    bits = []
    for name, size in axis_sizes:
        mask = 1
        while mask < size:
            bits.append((name, size, mask))
            mask *= 2
    return bits


def partner(x, name, size, mask):
    return lax.ppermute(x, name, [(i, i ^ mask) for i in range(size)])


def tree_sum(x, bits, halving):
    for name, size, mask in bits[:halving]:
        half = x.shape[0] // 2
        bit = (lax.axis_index(name) // mask) % 2
        keep = lax.dynamic_slice_in_dim(x, bit * half, half, 0)
        send = lax.dynamic_slice_in_dim(x, (1 - bit) * half, half, 0)
        x = keep + partner(send, name, size, mask)
    for name, size, mask in bits[halving:]:
        x = x + partner(x, name, size, mask)
    for name, size, mask in reversed(bits[:halving]):
        bit = (lax.axis_index(name) // mask) % 2
        other = partner(x, name, size, mask)
        x = jnp.where(bit == 0, jnp.concatenate([x, other]), jnp.concatenate([other, x]))
    return x


def peak_and_total(stats, bits):
    for name, size, mask in bits:
        other = partner(stats, name, size, mask)
        stats = jnp.concatenate(
            [jnp.maximum(stats[:1], other[:1]), stats[1:] + other[1:]], axis=0
        )
    return stats


def on_device(embeddings, projection, phase_code, penalty, assignment, targets):
    width = projection.shape[1]
    attrs = targets.shape[1]
    bits = exchange_bits([("docs", lax.axis_size("docs")), ("grp", lax.axis_size("grp"))])
    phases = phase_table(phase_code, width)
    projected = jnp.dot(embeddings, projection, preferred_element_type=jnp.float32)
    features = jnp.cos(projected + phases).astype(jnp.bfloat16)
    aligned = features[assignment.reshape(-1)]
    gram_part = lax.dot_general(
        features, features, (((0,), (0,)), ((), ())), preferred_element_type=jnp.float32
    )
    cross_part = lax.dot_general(
        aligned, targets, (((0,), (0,)), ((), ())), preferred_element_type=jnp.float32
    )
    block = 128
    nb = width // block
    lower_blocks = [
        gram_part[i * block:(i + 1) * block, j * block:(j + 1) * block]
        for i in range(nb)
        for j in range(i + 1)
    ]
    gram_flat = jnp.concatenate(lower_blocks, axis=0).reshape(-1, 128)
    gram_sum = tree_sum(gram_flat, bits, 3).reshape(len(lower_blocks), block, block)
    cross_bits = bits[:1] + bits[4:7] + bits[1:4] + bits[7:]
    cross = tree_sum(cross_part.reshape(-1, 128), cross_bits, 3).reshape(width, attrs)
    block_of = {}
    for n, (i, j) in enumerate((i, j) for i in range(nb) for j in range(i + 1)):
        block_of[(i, j)] = gram_sum[n]
        block_of[(j, i)] = gram_sum[n].T
    gram = jnp.concatenate(
        [jnp.concatenate([block_of[(i, j)] for j in range(nb)], axis=1) for i in range(nb)],
        axis=0,
    )
    total_rows = embeddings.shape[0] * lax.axis_size("docs") * lax.axis_size("grp")
    ridge_shift = penalty[0].astype(jnp.float32) * jnp.float32(total_rows / 8.0)
    system = gram + ridge_shift * jnp.eye(width, dtype=jnp.float32)
    factor = lax.linalg.cholesky(system, symmetrize_input=False)
    coeffs = jax.scipy.linalg.cho_solve((factor, True), cross).astype(jnp.bfloat16)
    scores = jnp.dot(features, coeffs, preferred_element_type=jnp.float32)
    peak_local = jnp.max(jnp.abs(scores), axis=0)
    column_sum = jnp.sum(scores, axis=0)
    stats = peak_and_total(jnp.stack([peak_local, column_sum]), bits)
    peak = stats[0]
    total = stats[1]
    quality = (scores - total / jnp.float32(total_rows)) / (peak + 1e-06)
    return quality.astype(jnp.bfloat16)


def solution(mesh):
    in_specs = (
        P(("docs", "grp"), None),
        P(),
        P(),
        P(),
        P(("docs", "grp"), None),
        P(("docs", "grp"), None),
    )
    out_specs = P(("docs", "grp"), None)
    return jax.shard_map(
        on_device, mesh=mesh, in_specs=in_specs, out_specs=out_specs, check_vma=False
    )
```

```python
import math

import jax
import jax.numpy as jnp
from jax import lax
from jax.sharding import PartitionSpec as P


def phase_table(phase_code, width):
    feature_ids = jnp.arange(width, dtype=jnp.int32)
    code_value = phase_code[0]
    index_value = (code_value * 389 + feature_ids * (feature_ids + code_value) * 53) % 4096
    return index_value.astype(jnp.float32) * (2.0 * math.pi / 4096.0)


def exchange_bits(axis_sizes):
    bits = []
    for name, size in axis_sizes:
        mask = 1
        while mask < size:
            bits.append((name, size, mask))
            mask *= 2
    return bits


def partner(x, name, size, mask):
    return lax.ppermute(x, name, [(i, i ^ mask) for i in range(size)])


def tree_sum(x, bits, halving):
    for name, size, mask in bits[:halving]:
        half = x.shape[0] // 2
        bit = (lax.axis_index(name) // mask) % 2
        keep = lax.dynamic_slice_in_dim(x, bit * half, half, 0)
        send = lax.dynamic_slice_in_dim(x, (1 - bit) * half, half, 0)
        x = keep + partner(send, name, size, mask)
    for name, size, mask in bits[halving:]:
        x = x + partner(x, name, size, mask)
    for name, size, mask in reversed(bits[:halving]):
        bit = (lax.axis_index(name) // mask) % 2
        other = partner(x, name, size, mask)
        x = jnp.where(bit == 0, jnp.concatenate([x, other]), jnp.concatenate([other, x]))
    return x


def peak_and_total(stats, bits):
    for name, size, mask in bits:
        other = partner(stats, name, size, mask)
        stats = jnp.concatenate(
            [jnp.maximum(stats[:1], other[:1]), stats[1:] + other[1:]], axis=0
        )
    return stats


def on_device(embeddings, projection, phase_code, penalty, assignment, targets):
    width = projection.shape[1]
    attrs = targets.shape[1]
    bits = exchange_bits([("docs", lax.axis_size("docs")), ("grp", lax.axis_size("grp"))])
    phases = phase_table(phase_code, width)
    projected = jnp.dot(embeddings, projection, preferred_element_type=jnp.float32)
    features = jnp.cos(projected + phases).astype(jnp.bfloat16)
    aligned = features[assignment.reshape(-1)]
    gram_part = lax.dot_general(
        features, features, (((0,), (0,)), ((), ())), preferred_element_type=jnp.float32
    )
    cross_part = lax.dot_general(
        aligned, targets, (((0,), (0,)), ((), ())), preferred_element_type=jnp.float32
    )
    block = 128
    nb = width // block
    lower_blocks = [
        gram_part[i * block:(i + 1) * block, j * block:(j + 1) * block]
        for i in range(nb)
        for j in range(i + 1)
    ]
    gram_flat = jnp.concatenate(lower_blocks, axis=0).reshape(-1, 128)
    cross_flat = cross_part.reshape(-1, 128)
    chip_bits = bits[1:]
    orders = [chip_bits[k:] + chip_bits[:k] for k in (0, 3, 6, 5)]
    pieces = []
    for n, part in enumerate(jnp.split(gram_flat, 2) + jnp.split(cross_flat, 2)):
        pieces.append(tree_sum(part, bits[:1] + orders[n], 3))
    gram_sum = jnp.concatenate(pieces[:2]).reshape(len(lower_blocks), block, block)
    cross = jnp.concatenate(pieces[2:]).reshape(width, attrs)
    block_of = {}
    for n, (i, j) in enumerate((i, j) for i in range(nb) for j in range(i + 1)):
        block_of[(i, j)] = gram_sum[n]
        block_of[(j, i)] = gram_sum[n].T
    gram = jnp.concatenate(
        [jnp.concatenate([block_of[(i, j)] for j in range(nb)], axis=1) for i in range(nb)],
        axis=0,
    )
    total_rows = embeddings.shape[0] * lax.axis_size("docs") * lax.axis_size("grp")
    ridge_shift = penalty[0].astype(jnp.float32) * jnp.float32(total_rows / 8.0)
    system = gram + ridge_shift * jnp.eye(width, dtype=jnp.float32)
    factor = lax.linalg.cholesky(system, symmetrize_input=False)
    coeffs = jax.scipy.linalg.cho_solve((factor, True), cross).astype(jnp.bfloat16)
    scores = jnp.dot(features, coeffs, preferred_element_type=jnp.float32)
    peak_local = jnp.max(jnp.abs(scores), axis=0)
    column_sum = jnp.sum(scores, axis=0)
    stats = peak_and_total(jnp.stack([peak_local, column_sum]), bits)
    peak = stats[0]
    total = stats[1]
    quality = (scores - total / jnp.float32(total_rows)) / (peak + 1e-06)
    return quality.astype(jnp.bfloat16)


def solution(mesh):
    in_specs = (
        P(("docs", "grp"), None),
        P(),
        P(),
        P(),
        P(("docs", "grp"), None),
        P(("docs", "grp"), None),
    )
    out_specs = P(("docs", "grp"), None)
    return jax.shard_map(
        on_device, mesh=mesh, in_specs=in_specs, out_specs=out_specs, check_vma=False
    )
```

```python
import math

import jax
import jax.numpy as jnp
from jax import lax
from jax.sharding import PartitionSpec as P


def phase_table(phase_code, width):
    feature_ids = jnp.arange(width, dtype=jnp.int32)
    code_value = phase_code[0]
    index_value = (code_value * 389 + feature_ids * (feature_ids + code_value) * 53) % 4096
    return index_value.astype(jnp.float32) * (2.0 * math.pi / 4096.0)


def exchange_bits(axis_sizes):
    bits = []
    for name, size in axis_sizes:
        mask = 1
        while mask < size:
            bits.append((name, size, mask))
            mask *= 2
    return bits


def partner(x, name, size, mask):
    return lax.ppermute(x, name, [(i, i ^ mask) for i in range(size)])


def tree_sum(x, bits, halving):
    for name, size, mask in bits[:halving]:
        half = x.shape[0] // 2
        bit = (lax.axis_index(name) // mask) % 2
        keep = lax.dynamic_slice_in_dim(x, bit * half, half, 0)
        send = lax.dynamic_slice_in_dim(x, (1 - bit) * half, half, 0)
        x = keep + partner(send, name, size, mask)
    for name, size, mask in bits[halving:]:
        x = x + partner(x, name, size, mask)
    for name, size, mask in reversed(bits[:halving]):
        bit = (lax.axis_index(name) // mask) % 2
        other = partner(x, name, size, mask)
        x = jnp.where(bit == 0, jnp.concatenate([x, other]), jnp.concatenate([other, x]))
    return x


def peak_and_total(stats, bits):
    for name, size, mask in bits:
        other = partner(stats, name, size, mask)
        stats = jnp.concatenate(
            [jnp.maximum(stats[:1], other[:1]), stats[1:] + other[1:]], axis=0
        )
    return stats


def on_device(embeddings, projection, phase_code, penalty, assignment, targets):
    width = projection.shape[1]
    attrs = targets.shape[1]
    bits = exchange_bits([("docs", lax.axis_size("docs")), ("grp", lax.axis_size("grp"))])
    phases = phase_table(phase_code, width)
    projected = jnp.dot(embeddings, projection, preferred_element_type=jnp.float32)
    features = jnp.cos(projected + phases).astype(jnp.bfloat16)
    aligned = features[assignment.reshape(-1)]
    gram_part = lax.dot_general(
        features, features, (((0,), (0,)), ((), ())), preferred_element_type=jnp.float32
    )
    cross_part = lax.dot_general(
        aligned, targets, (((0,), (0,)), ((), ())), preferred_element_type=jnp.float32
    )
    block = 128
    nb = width // block
    lower_blocks = [
        gram_part[i * block:(i + 1) * block, j * block:(j + 1) * block]
        for i in range(nb)
        for j in range(i + 1)
    ]
    gram_flat = jnp.concatenate(lower_blocks, axis=0).reshape(-1, 128)
    gram_sum = tree_sum(gram_flat, bits, 1).reshape(len(lower_blocks), block, block)
    cross_bits = bits[:1] + bits[4:7] + bits[1:4] + bits[7:]
    cross = tree_sum(cross_part.reshape(-1, 128), cross_bits, 1).reshape(width, attrs)
    block_of = {}
    for n, (i, j) in enumerate((i, j) for i in range(nb) for j in range(i + 1)):
        block_of[(i, j)] = gram_sum[n]
        block_of[(j, i)] = gram_sum[n].T
    gram = jnp.concatenate(
        [jnp.concatenate([block_of[(i, j)] for j in range(nb)], axis=1) for i in range(nb)],
        axis=0,
    )
    total_rows = embeddings.shape[0] * lax.axis_size("docs") * lax.axis_size("grp")
    ridge_shift = penalty[0].astype(jnp.float32) * jnp.float32(total_rows / 8.0)
    system = gram + ridge_shift * jnp.eye(width, dtype=jnp.float32)
    factor = lax.linalg.cholesky(system, symmetrize_input=False)
    coeffs = jax.scipy.linalg.cho_solve((factor, True), cross).astype(jnp.bfloat16)
    scores = jnp.dot(features, coeffs, preferred_element_type=jnp.float32)
    peak_local = jnp.max(jnp.abs(scores), axis=0)
    column_sum = jnp.sum(scores, axis=0)
    stats = peak_and_total(jnp.stack([peak_local, column_sum]), bits)
    peak = stats[0]
    total = stats[1]
    quality = (scores - total / jnp.float32(total_rows)) / (peak + 1e-06)
    return quality.astype(jnp.bfloat16)


def solution(mesh):
    in_specs = (
        P(("docs", "grp"), None),
        P(),
        P(),
        P(),
        P(("docs", "grp"), None),
        P(("docs", "grp"), None),
    )
    out_specs = P(("docs", "grp"), None)
    return jax.shard_map(
        on_device, mesh=mesh, in_specs=in_specs, out_specs=out_specs, check_vma=False
    )
```

```python
import math

import jax
import jax.numpy as jnp
from jax import lax
from jax.sharding import PartitionSpec as P


def phase_table(phase_code, width):
    feature_ids = jnp.arange(width, dtype=jnp.int32)
    code_value = phase_code[0]
    index_value = (code_value * 389 + feature_ids * (feature_ids + code_value) * 53) % 4096
    return index_value.astype(jnp.float32) * (2.0 * math.pi / 4096.0)


def exchange_bits(axis_sizes):
    bits = []
    for name, size in axis_sizes:
        mask = 1
        while mask < size:
            bits.append((name, size, mask))
            mask *= 2
    return bits


def partner(x, name, size, mask):
    return lax.ppermute(x, name, [(i, i ^ mask) for i in range(size)])


def tree_sum(x, bits, halving):
    for name, size, mask in bits[:halving]:
        half = x.shape[0] // 2
        bit = (lax.axis_index(name) // mask) % 2
        keep = lax.dynamic_slice_in_dim(x, bit * half, half, 0)
        send = lax.dynamic_slice_in_dim(x, (1 - bit) * half, half, 0)
        x = keep + partner(send, name, size, mask)
    for name, size, mask in bits[halving:]:
        x = x + partner(x, name, size, mask)
    for name, size, mask in reversed(bits[:halving]):
        bit = (lax.axis_index(name) // mask) % 2
        other = partner(x, name, size, mask)
        x = jnp.where(bit == 0, jnp.concatenate([x, other]), jnp.concatenate([other, x]))
    return x


def peak_and_total(stats, bits):
    for name, size, mask in bits:
        other = partner(stats, name, size, mask)
        stats = jnp.concatenate(
            [jnp.maximum(stats[:1], other[:1]), stats[1:] + other[1:]], axis=0
        )
    return stats


HIGHEST = lax.Precision.HIGHEST


def diagonal_block_inverses(factor, block):
    count = factor.shape[0] // block
    diag = jnp.stack(
        [factor[k * block:(k + 1) * block, k * block:(k + 1) * block] for k in range(count)]
    )
    pivots = jnp.diagonal(diag, axis1=1, axis2=2)
    eye = jnp.eye(block, dtype=factor.dtype)
    power = eye - diag / pivots[:, :, None]
    product = eye + power
    reach = 2
    while reach < block:
        power = jnp.einsum("kij,kjl->kil", power, power, precision=HIGHEST)
        product = jnp.einsum("kij,kjl->kil", product, eye + power, precision=HIGHEST)
        reach *= 2
    return product / pivots[:, None, :]


def cholesky_solve(factor, rhs, block):
    count = factor.shape[0] // block
    inverses = diagonal_block_inverses(factor, block)
    forward = []
    for k in range(count):
        rows = slice(k * block, (k + 1) * block)
        residual = rhs[rows]
        if k:
            residual = residual - jnp.dot(
                factor[rows, :k * block], jnp.concatenate(forward), precision=HIGHEST
            )
        forward.append(jnp.dot(inverses[k], residual, precision=HIGHEST))
    backward = [None] * count
    for k in reversed(range(count)):
        residual = forward[k]
        if k < count - 1:
            below = factor[(k + 1) * block:, k * block:(k + 1) * block]
            residual = residual - jnp.dot(
                below.T, jnp.concatenate(backward[k + 1:]), precision=HIGHEST
            )
        backward[k] = jnp.dot(inverses[k].T, residual, precision=HIGHEST)
    return jnp.concatenate(backward)


def on_device(embeddings, projection, phase_code, penalty, assignment, targets):
    width = projection.shape[1]
    attrs = targets.shape[1]
    bits = exchange_bits([("docs", lax.axis_size("docs")), ("grp", lax.axis_size("grp"))])
    phases = phase_table(phase_code, width)
    projected = jnp.dot(embeddings, projection, preferred_element_type=jnp.float32)
    features = jnp.cos(projected + phases).astype(jnp.bfloat16)
    aligned = features[assignment.reshape(-1)]
    gram_part = lax.dot_general(
        features, features, (((0,), (0,)), ((), ())), preferred_element_type=jnp.float32
    )
    cross_part = lax.dot_general(
        aligned, targets, (((0,), (0,)), ((), ())), preferred_element_type=jnp.float32
    )
    block = 128
    nb = width // block
    lower_blocks = [
        gram_part[i * block:(i + 1) * block, j * block:(j + 1) * block]
        for i in range(nb)
        for j in range(i + 1)
    ]
    gram_flat = jnp.concatenate(lower_blocks, axis=0).reshape(-1, 128)
    gram_sum = tree_sum(gram_flat, bits, 3).reshape(len(lower_blocks), block, block)
    cross_bits = bits[:1] + bits[4:7] + bits[1:4] + bits[7:]
    cross = tree_sum(cross_part.reshape(-1, 128), cross_bits, 3).reshape(width, attrs)
    block_of = {}
    for n, (i, j) in enumerate((i, j) for i in range(nb) for j in range(i + 1)):
        block_of[(i, j)] = gram_sum[n]
        block_of[(j, i)] = gram_sum[n].T
    gram = jnp.concatenate(
        [jnp.concatenate([block_of[(i, j)] for j in range(nb)], axis=1) for i in range(nb)],
        axis=0,
    )
    total_rows = embeddings.shape[0] * lax.axis_size("docs") * lax.axis_size("grp")
    ridge_shift = penalty[0].astype(jnp.float32) * jnp.float32(total_rows / 8.0)
    system = gram + ridge_shift * jnp.eye(width, dtype=jnp.float32)
    factor = lax.linalg.cholesky(system, symmetrize_input=False)
    coeffs = cholesky_solve(factor, cross, 64).astype(jnp.bfloat16)
    scores = jnp.dot(features, coeffs, preferred_element_type=jnp.float32)
    peak_local = jnp.max(jnp.abs(scores), axis=0)
    column_sum = jnp.sum(scores, axis=0)
    stats = peak_and_total(jnp.stack([peak_local, column_sum]), bits)
    peak = stats[0]
    total = stats[1]
    quality = (scores - total / jnp.float32(total_rows)) / (peak + 1e-06)
    return quality.astype(jnp.bfloat16)


def solution(mesh):
    in_specs = (
        P(("docs", "grp"), None),
        P(),
        P(),
        P(),
        P(("docs", "grp"), None),
        P(("docs", "grp"), None),
    )
    out_specs = P(("docs", "grp"), None)
    return jax.shard_map(
        on_device, mesh=mesh, in_specs=in_specs, out_specs=out_specs, check_vma=False
    )
```

```python
import math

import jax
import jax.numpy as jnp
from jax import lax
from jax.sharding import PartitionSpec as P


def phase_table(phase_code, width):
    feature_ids = jnp.arange(width, dtype=jnp.int32)
    code_value = phase_code[0]
    index_value = (code_value * 389 + feature_ids * (feature_ids + code_value) * 53) % 4096
    return index_value.astype(jnp.float32) * (2.0 * math.pi / 4096.0)


def exchange_bits(axis_sizes):
    bits = []
    for name, size in axis_sizes:
        mask = 1
        while mask < size:
            bits.append((name, size, mask))
            mask *= 2
    return bits


def partner(x, name, size, mask):
    return lax.ppermute(x, name, [(i, i ^ mask) for i in range(size)])


def tree_sum(x, bits, halving):
    for name, size, mask in bits[:halving]:
        half = x.shape[0] // 2
        bit = (lax.axis_index(name) // mask) % 2
        keep = lax.dynamic_slice_in_dim(x, bit * half, half, 0)
        send = lax.dynamic_slice_in_dim(x, (1 - bit) * half, half, 0)
        x = keep + partner(send, name, size, mask)
    for name, size, mask in bits[halving:]:
        x = x + partner(x, name, size, mask)
    for name, size, mask in reversed(bits[:halving]):
        bit = (lax.axis_index(name) // mask) % 2
        other = partner(x, name, size, mask)
        x = jnp.where(bit == 0, jnp.concatenate([x, other]), jnp.concatenate([other, x]))
    return x


def peak_and_total(stats, bits):
    for name, size, mask in bits:
        other = partner(stats, name, size, mask)
        stats = jnp.concatenate(
            [jnp.maximum(stats[:1], other[:1]), stats[1:] + other[1:]], axis=0
        )
    return stats


HIGHEST = lax.Precision.HIGHEST


def triangular_inverse(lower):
    size = lower.shape[0]
    pivots = jnp.diagonal(lower)
    eye = jnp.eye(size, dtype=lower.dtype)
    power = eye - lower / pivots[:, None]
    product = eye + power
    reach = 2
    while reach < size:
        power = jnp.dot(power, power, precision=HIGHEST)
        product = jnp.dot(product, eye + power, precision=HIGHEST)
        reach *= 2
    return product / pivots[None, :]


def blocked_cholesky(system, block):
    count = system.shape[0] // block
    trailing = system
    columns = []
    inverses = []
    for k in range(count):
        head = lax.linalg.cholesky(trailing[:block, :block], symmetrize_input=False)
        inverse = triangular_inverse(head)
        inverses.append(inverse)
        above = [jnp.zeros((k * block, block), system.dtype)] if k else []
        if k < count - 1:
            panel = jnp.dot(trailing[block:, :block], inverse.T, precision=HIGHEST)
            trailing = trailing[block:, block:] - jnp.dot(panel, panel.T, precision=HIGHEST)
            columns.append(jnp.concatenate(above + [head, panel]))
        else:
            columns.append(jnp.concatenate(above + [head]))
    return jnp.concatenate(columns, axis=1), inverses


def cholesky_solve(factor, inverses, rhs, block):
    count = factor.shape[0] // block
    forward = []
    for k in range(count):
        rows = slice(k * block, (k + 1) * block)
        residual = rhs[rows]
        if k:
            residual = residual - jnp.dot(
                factor[rows, :k * block], jnp.concatenate(forward), precision=HIGHEST
            )
        forward.append(jnp.dot(inverses[k], residual, precision=HIGHEST))
    backward = [None] * count
    for k in reversed(range(count)):
        residual = forward[k]
        if k < count - 1:
            below = factor[(k + 1) * block:, k * block:(k + 1) * block]
            residual = residual - jnp.dot(
                below.T, jnp.concatenate(backward[k + 1:]), precision=HIGHEST
            )
        backward[k] = jnp.dot(inverses[k].T, residual, precision=HIGHEST)
    return jnp.concatenate(backward)


def on_device(embeddings, projection, phase_code, penalty, assignment, targets):
    width = projection.shape[1]
    attrs = targets.shape[1]
    bits = exchange_bits([("docs", lax.axis_size("docs")), ("grp", lax.axis_size("grp"))])
    phases = phase_table(phase_code, width)
    projected = jnp.dot(embeddings, projection, preferred_element_type=jnp.float32)
    features = jnp.cos(projected + phases).astype(jnp.bfloat16)
    aligned = features[assignment.reshape(-1)]
    gram_part = lax.dot_general(
        features, features, (((0,), (0,)), ((), ())), preferred_element_type=jnp.float32
    )
    cross_part = lax.dot_general(
        aligned, targets, (((0,), (0,)), ((), ())), preferred_element_type=jnp.float32
    )
    block = 128
    nb = width // block
    lower_blocks = [
        gram_part[i * block:(i + 1) * block, j * block:(j + 1) * block]
        for i in range(nb)
        for j in range(i + 1)
    ]
    gram_flat = jnp.concatenate(lower_blocks, axis=0).reshape(-1, 128)
    gram_sum = tree_sum(gram_flat, bits, 3).reshape(len(lower_blocks), block, block)
    cross_bits = bits[:1] + bits[4:7] + bits[1:4] + bits[7:]
    cross = tree_sum(cross_part.reshape(-1, 128), cross_bits, 3).reshape(width, attrs)
    block_of = {}
    for n, (i, j) in enumerate((i, j) for i in range(nb) for j in range(i + 1)):
        block_of[(i, j)] = gram_sum[n]
        block_of[(j, i)] = gram_sum[n].T
    gram = jnp.concatenate(
        [jnp.concatenate([block_of[(i, j)] for j in range(nb)], axis=1) for i in range(nb)],
        axis=0,
    )
    total_rows = embeddings.shape[0] * lax.axis_size("docs") * lax.axis_size("grp")
    ridge_shift = penalty[0].astype(jnp.float32) * jnp.float32(total_rows / 8.0)
    system = gram + ridge_shift * jnp.eye(width, dtype=jnp.float32)
    factor, inverses = blocked_cholesky(system, block)
    coeffs = cholesky_solve(factor, inverses, cross, block).astype(jnp.bfloat16)
    scores = jnp.dot(features, coeffs, preferred_element_type=jnp.float32)
    peak_local = jnp.max(jnp.abs(scores), axis=0)
    column_sum = jnp.sum(scores, axis=0)
    stats = peak_and_total(jnp.stack([peak_local, column_sum]), bits)
    peak = stats[0]
    total = stats[1]
    quality = (scores - total / jnp.float32(total_rows)) / (peak + 1e-06)
    return quality.astype(jnp.bfloat16)


def solution(mesh):
    in_specs = (
        P(("docs", "grp"), None),
        P(),
        P(),
        P(),
        P(("docs", "grp"), None),
        P(("docs", "grp"), None),
    )
    out_specs = P(("docs", "grp"), None)
    return jax.shard_map(
        on_device, mesh=mesh, in_specs=in_specs, out_specs=out_specs, check_vma=False
    )
```

```python
import math

import jax
import jax.numpy as jnp
from jax import lax
from jax.sharding import PartitionSpec as P


def phase_table(phase_code, width):
    feature_ids = jnp.arange(width, dtype=jnp.int32)
    code_value = phase_code[0]
    index_value = (code_value * 389 + feature_ids * (feature_ids + code_value) * 53) % 4096
    return index_value.astype(jnp.float32) * (2.0 * math.pi / 4096.0)


def exchange_bits(axis_sizes):
    bits = []
    for name, size in axis_sizes:
        mask = 1
        while mask < size:
            bits.append((name, size, mask))
            mask *= 2
    return bits


def partner(x, name, size, mask):
    return lax.ppermute(x, name, [(i, i ^ mask) for i in range(size)])


def tree_sum(x, bits, halving):
    for name, size, mask in bits[:halving]:
        half = x.shape[0] // 2
        bit = (lax.axis_index(name) // mask) % 2
        keep = lax.dynamic_slice_in_dim(x, bit * half, half, 0)
        send = lax.dynamic_slice_in_dim(x, (1 - bit) * half, half, 0)
        x = keep + partner(send, name, size, mask)
    for name, size, mask in bits[halving:]:
        x = x + partner(x, name, size, mask)
    for name, size, mask in reversed(bits[:halving]):
        bit = (lax.axis_index(name) // mask) % 2
        other = partner(x, name, size, mask)
        x = jnp.where(bit == 0, jnp.concatenate([x, other]), jnp.concatenate([other, x]))
    return x


def peak_and_total(stats, bits):
    for name, size, mask in bits:
        other = partner(stats, name, size, mask)
        stats = jnp.concatenate(
            [jnp.maximum(stats[:1], other[:1]), stats[1:] + other[1:]], axis=0
        )
    return stats


HIGHEST = lax.Precision.HIGHEST


def triangular_inverse(lower):
    size = lower.shape[0]
    eye = jnp.eye(size, dtype=lower.dtype)
    pivots = jnp.sum(lower * eye, axis=1)
    power = eye - lower / pivots[:, None]
    product = eye + power
    reach = 2
    while reach < size:
        power = jnp.dot(power, power, precision=HIGHEST)
        product = jnp.dot(product, eye + power, precision=HIGHEST)
        reach *= 2
    return product / pivots[None, :]


def blocked_cholesky(system, block):
    count = system.shape[0] // block
    trailing = system
    columns = []
    inverses = []
    for k in range(count):
        head = lax.linalg.cholesky(trailing[:block, :block], symmetrize_input=False)
        inverse = triangular_inverse(head)
        inverses.append(inverse)
        above = [jnp.zeros((k * block, block), system.dtype)] if k else []
        if k < count - 1:
            panel = jnp.dot(trailing[block:, :block], inverse.T, precision=HIGHEST)
            trailing = trailing[block:, block:] - jnp.dot(panel, panel.T, precision=HIGHEST)
            columns.append(jnp.concatenate(above + [head, panel]))
        else:
            columns.append(jnp.concatenate(above + [head]))
    return jnp.concatenate(columns, axis=1), inverses


def cholesky_solve(factor, inverses, rhs, block):
    count = factor.shape[0] // block
    forward = []
    for k in range(count):
        rows = slice(k * block, (k + 1) * block)
        residual = rhs[rows]
        if k:
            residual = residual - jnp.dot(
                factor[rows, :k * block], jnp.concatenate(forward), precision=HIGHEST
            )
        forward.append(jnp.dot(inverses[k], residual, precision=HIGHEST))
    backward = [None] * count
    for k in reversed(range(count)):
        residual = forward[k]
        if k < count - 1:
            below = factor[(k + 1) * block:, k * block:(k + 1) * block]
            residual = residual - jnp.dot(
                below.T, jnp.concatenate(backward[k + 1:]), precision=HIGHEST
            )
        backward[k] = jnp.dot(inverses[k].T, residual, precision=HIGHEST)
    return jnp.concatenate(backward)


def on_device(embeddings, projection, phase_code, penalty, assignment, targets):
    width = projection.shape[1]
    attrs = targets.shape[1]
    bits = exchange_bits([("docs", lax.axis_size("docs")), ("grp", lax.axis_size("grp"))])
    phases = phase_table(phase_code, width)
    projected = jnp.dot(embeddings, projection, preferred_element_type=jnp.float32)
    features = jnp.cos(projected + phases).astype(jnp.bfloat16)
    aligned = features[assignment.reshape(-1)]
    gram_part = lax.dot_general(
        features, features, (((0,), (0,)), ((), ())), preferred_element_type=jnp.float32
    )
    cross_part = lax.dot_general(
        aligned, targets, (((0,), (0,)), ((), ())), preferred_element_type=jnp.float32
    )
    block = 128
    nb = width // block
    lower_blocks = [
        gram_part[i * block:(i + 1) * block, j * block:(j + 1) * block]
        for i in range(nb)
        for j in range(i + 1)
    ]
    gram_flat = jnp.concatenate(lower_blocks, axis=0).reshape(-1, 128)
    gram_sum = tree_sum(gram_flat, bits, 3).reshape(len(lower_blocks), block, block)
    cross_bits = bits[:1] + bits[4:7] + bits[1:4] + bits[7:]
    cross = tree_sum(cross_part.reshape(-1, 128), cross_bits, 3).reshape(width, attrs)
    block_of = {}
    for n, (i, j) in enumerate((i, j) for i in range(nb) for j in range(i + 1)):
        block_of[(i, j)] = gram_sum[n]
        block_of[(j, i)] = gram_sum[n].T
    gram = jnp.concatenate(
        [jnp.concatenate([block_of[(i, j)] for j in range(nb)], axis=1) for i in range(nb)],
        axis=0,
    )
    total_rows = embeddings.shape[0] * lax.axis_size("docs") * lax.axis_size("grp")
    ridge_shift = penalty[0].astype(jnp.float32) * jnp.float32(total_rows / 8.0)
    system = gram + ridge_shift * jnp.eye(width, dtype=jnp.float32)
    factor, inverses = blocked_cholesky(system, block)
    coeffs = cholesky_solve(factor, inverses, cross, block).astype(jnp.bfloat16)
    scores = jnp.dot(features, coeffs, preferred_element_type=jnp.float32)
    peak_local = jnp.max(jnp.abs(scores), axis=0)
    column_sum = jnp.sum(scores, axis=0)
    stats = peak_and_total(jnp.stack([peak_local, column_sum]), bits)
    peak = stats[0]
    total = stats[1]
    quality = (scores - total / jnp.float32(total_rows)) / (peak + 1e-06)
    return quality.astype(jnp.bfloat16)


def solution(mesh):
    in_specs = (
        P(("docs", "grp"), None),
        P(),
        P(),
        P(),
        P(("docs", "grp"), None),
        P(("docs", "grp"), None),
    )
    out_specs = P(("docs", "grp"), None)
    return jax.shard_map(
        on_device, mesh=mesh, in_specs=in_specs, out_specs=out_specs, check_vma=False
    )
```

```python
import math

import jax
import jax.numpy as jnp
from jax import lax
from jax.sharding import PartitionSpec as P


def phase_table(phase_code, width):
    feature_ids = jnp.arange(width, dtype=jnp.int32)
    code_value = phase_code[0]
    index_value = (code_value * 389 + feature_ids * (feature_ids + code_value) * 53) % 4096
    return index_value.astype(jnp.float32) * (2.0 * math.pi / 4096.0)


def exchange_bits(axis_sizes):
    bits = []
    for name, size in axis_sizes:
        mask = 1
        while mask < size:
            bits.append((name, size, mask))
            mask *= 2
    return bits


def partner(x, name, size, mask):
    return lax.ppermute(x, name, [(i, i ^ mask) for i in range(size)])


def tree_sum(x, bits, halving):
    for name, size, mask in bits[:halving]:
        half = x.shape[0] // 2
        bit = (lax.axis_index(name) // mask) % 2
        keep = lax.dynamic_slice_in_dim(x, bit * half, half, 0)
        send = lax.dynamic_slice_in_dim(x, (1 - bit) * half, half, 0)
        x = keep + partner(send, name, size, mask)
    for name, size, mask in bits[halving:]:
        x = x + partner(x, name, size, mask)
    for name, size, mask in reversed(bits[:halving]):
        bit = (lax.axis_index(name) // mask) % 2
        other = partner(x, name, size, mask)
        x = jnp.where(bit == 0, jnp.concatenate([x, other]), jnp.concatenate([other, x]))
    return x


def peak_and_total(stats, bits):
    for name, size, mask in bits:
        other = partner(stats, name, size, mask)
        stats = jnp.concatenate(
            [jnp.maximum(stats[:1], other[:1]), stats[1:] + other[1:]], axis=0
        )
    return stats


HIGHEST = lax.Precision.HIGHEST


def triangular_inverse(lower):
    size = lower.shape[0]
    eye = jnp.eye(size, dtype=lower.dtype)
    pivots = jnp.sum(lower * eye, axis=1)
    power = eye - lower / pivots[:, None]
    product = eye + power
    reach = 2
    while reach < size:
        power = jnp.dot(power, power, precision=HIGHEST)
        product = jnp.dot(product, eye + power, precision=HIGHEST)
        reach *= 2
    return product / pivots[None, :]


def blocked_cholesky(system, block):
    count = system.shape[0] // block
    trailing = system
    columns = []
    inverses = []
    for k in range(count):
        head = lax.linalg.cholesky(trailing[:block, :block], symmetrize_input=False)
        inverse = triangular_inverse(head)
        inverses.append(inverse)
        above = [jnp.zeros((k * block, block), system.dtype)] if k else []
        if k < count - 1:
            panel = jnp.dot(trailing[block:, :block], inverse.T, precision=HIGHEST)
            trailing = trailing[block:, block:] - jnp.dot(panel, panel.T, precision=HIGHEST)
            columns.append(jnp.concatenate(above + [head, panel]))
        else:
            columns.append(jnp.concatenate(above + [head]))
    return jnp.concatenate(columns, axis=1), inverses


def cholesky_solve(factor, inverses, rhs, block):
    count = factor.shape[0] // block
    forward = []
    for k in range(count):
        rows = slice(k * block, (k + 1) * block)
        residual = rhs[rows]
        if k:
            residual = residual - jnp.dot(
                factor[rows, :k * block], jnp.concatenate(forward), precision=HIGHEST
            )
        forward.append(jnp.dot(inverses[k], residual, precision=HIGHEST))
    backward = [None] * count
    for k in reversed(range(count)):
        residual = forward[k]
        if k < count - 1:
            below = factor[(k + 1) * block:, k * block:(k + 1) * block]
            residual = residual - jnp.dot(
                below.T, jnp.concatenate(backward[k + 1:]), precision=HIGHEST
            )
        backward[k] = jnp.dot(inverses[k].T, residual, precision=HIGHEST)
    return jnp.concatenate(backward)


def on_device(embeddings, projection, phase_code, penalty, assignment, targets):
    width = projection.shape[1]
    attrs = targets.shape[1]
    bits = exchange_bits([("docs", lax.axis_size("docs")), ("grp", lax.axis_size("grp"))])
    phases = phase_table(phase_code, width)
    projected = jnp.dot(embeddings, projection, preferred_element_type=jnp.float32)
    features = jnp.cos(projected + phases).astype(jnp.bfloat16)
    aligned = features[assignment.reshape(-1)]
    gram_part = lax.dot_general(
        features, features, (((0,), (0,)), ((), ())), preferred_element_type=jnp.float32
    )
    cross_part = lax.dot_general(
        aligned, targets, (((0,), (0,)), ((), ())), preferred_element_type=jnp.float32
    )
    block = 128
    nb = width // block
    lower_blocks = [
        gram_part[i * block:(i + 1) * block, j * block:(j + 1) * block]
        for i in range(nb)
        for j in range(i + 1)
    ]
    gram_flat = jnp.concatenate(lower_blocks, axis=0).reshape(-1, 128)
    gram_sum = tree_sum(gram_flat, bits, 3).reshape(len(lower_blocks), block, block)
    cross_bits = bits[:1] + bits[4:7] + bits[1:4] + bits[7:]
    cross = tree_sum(cross_part.reshape(-1, 128), cross_bits, 3).reshape(width, attrs)
    block_of = {}
    for n, (i, j) in enumerate((i, j) for i in range(nb) for j in range(i + 1)):
        block_of[(i, j)] = gram_sum[n]
        block_of[(j, i)] = gram_sum[n].T
    gram = jnp.concatenate(
        [jnp.concatenate([block_of[(i, j)] for j in range(nb)], axis=1) for i in range(nb)],
        axis=0,
    )
    total_rows = embeddings.shape[0] * lax.axis_size("docs") * lax.axis_size("grp")
    ridge_shift = penalty[0].astype(jnp.float32) * jnp.float32(total_rows / 8.0)
    system = gram + ridge_shift * jnp.eye(width, dtype=jnp.float32)
    factor, inverses = blocked_cholesky(system, block)
    coeffs = cholesky_solve(factor, inverses, cross, block).astype(jnp.bfloat16)
    scores = jnp.dot(features, coeffs, preferred_element_type=jnp.float32)
    peak_local = jnp.max(jnp.abs(scores), axis=0)
    column_sum = jnp.sum(scores, axis=0)
    stats = peak_and_total(jnp.stack([peak_local, column_sum]), bits[::-1])
    peak = stats[0]
    total = stats[1]
    quality = (scores - total / jnp.float32(total_rows)) / (peak + 1e-06)
    return quality.astype(jnp.bfloat16)


def solution(mesh):
    in_specs = (
        P(("docs", "grp"), None),
        P(),
        P(),
        P(),
        P(("docs", "grp"), None),
        P(("docs", "grp"), None),
    )
    out_specs = P(("docs", "grp"), None)
    return jax.shard_map(
        on_device, mesh=mesh, in_specs=in_specs, out_specs=out_specs, check_vma=False
    )
```

```python
import math

import jax
import jax.numpy as jnp
from jax import lax
from jax.sharding import PartitionSpec as P


def phase_table(phase_code, width):
    feature_ids = jnp.arange(width, dtype=jnp.int32)
    code_value = phase_code[0]
    index_value = (code_value * 389 + feature_ids * (feature_ids + code_value) * 53) % 4096
    return index_value.astype(jnp.float32) * (2.0 * math.pi / 4096.0)


def exchange_bits(axis_sizes):
    bits = []
    for name, size in axis_sizes:
        mask = 1
        while mask < size:
            bits.append((name, size, mask))
            mask *= 2
    return bits


def partner(x, name, size, mask):
    return lax.ppermute(x, name, [(i, i ^ mask) for i in range(size)])


def tree_sum(x, bits, halving):
    for name, size, mask in bits[:halving]:
        half = x.shape[0] // 2
        bit = (lax.axis_index(name) // mask) % 2
        keep = lax.dynamic_slice_in_dim(x, bit * half, half, 0)
        send = lax.dynamic_slice_in_dim(x, (1 - bit) * half, half, 0)
        x = keep + partner(send, name, size, mask)
    for name, size, mask in bits[halving:]:
        x = x + partner(x, name, size, mask)
    for name, size, mask in reversed(bits[:halving]):
        bit = (lax.axis_index(name) // mask) % 2
        other = partner(x, name, size, mask)
        x = jnp.where(bit == 0, jnp.concatenate([x, other]), jnp.concatenate([other, x]))
    return x


def peak_and_total(stats, bits):
    for name, size, mask in bits:
        other = partner(stats, name, size, mask)
        stats = jnp.concatenate(
            [jnp.maximum(stats[:1], other[:1]), stats[1:] + other[1:]], axis=0
        )
    return stats


HIGHEST = lax.Precision.HIGHEST


def triangular_inverse(lower):
    size = lower.shape[0]
    eye = jnp.eye(size, dtype=lower.dtype)
    pivots = jnp.sum(lower * eye, axis=1)
    power = eye - lower / pivots[:, None]
    product = eye + power
    reach = 2
    while reach < size:
        power = jnp.dot(power, power, precision=HIGHEST)
        product = jnp.dot(product, eye + power, precision=HIGHEST)
        reach *= 2
    return product / pivots[None, :]


def blocked_cholesky(system, block):
    count = system.shape[0] // block
    trailing = system
    columns = []
    inverses = []
    for k in range(count):
        head = lax.linalg.cholesky(trailing[:block, :block], symmetrize_input=False)
        inverse = triangular_inverse(head)
        inverses.append(inverse)
        above = [jnp.zeros((k * block, block), system.dtype)] if k else []
        if k < count - 1:
            panel = jnp.dot(trailing[block:, :block], inverse.T, precision=HIGHEST)
            trailing = trailing[block:, block:] - jnp.dot(panel, panel.T, precision=HIGHEST)
            columns.append(jnp.concatenate(above + [head, panel]))
        else:
            columns.append(jnp.concatenate(above + [head]))
    return jnp.concatenate(columns, axis=1), inverses


def cholesky_solve(factor, inverses, rhs, block):
    count = factor.shape[0] // block
    forward = []
    for k in range(count):
        rows = slice(k * block, (k + 1) * block)
        residual = rhs[rows]
        if k:
            residual = residual - jnp.dot(
                factor[rows, :k * block], jnp.concatenate(forward), precision=HIGHEST
            )
        forward.append(jnp.dot(inverses[k], residual, precision=HIGHEST))
    backward = [None] * count
    for k in reversed(range(count)):
        residual = forward[k]
        if k < count - 1:
            below = factor[(k + 1) * block:, k * block:(k + 1) * block]
            residual = residual - jnp.dot(
                below.T, jnp.concatenate(backward[k + 1:]), precision=HIGHEST
            )
        backward[k] = jnp.dot(inverses[k].T, residual, precision=HIGHEST)
    return jnp.concatenate(backward)


def on_device(embeddings, projection, phase_code, penalty, assignment, targets):
    width = projection.shape[1]
    attrs = targets.shape[1]
    bits = exchange_bits([("docs", lax.axis_size("docs")), ("grp", lax.axis_size("grp"))])
    phases = phase_table(phase_code, width)
    projected = jnp.dot(embeddings, projection, preferred_element_type=jnp.float32)
    features = jnp.cos(projected + phases).astype(jnp.bfloat16)
    aligned = features[assignment.reshape(-1)]
    gram_part = lax.dot_general(
        features, features, (((0,), (0,)), ((), ())), preferred_element_type=jnp.float32
    )
    cross_part = lax.dot_general(
        aligned, targets, (((0,), (0,)), ((), ())), preferred_element_type=jnp.float32
    )
    block = 128
    nb = width // block
    lower_blocks = [
        gram_part[i * block:(i + 1) * block, j * block:(j + 1) * block]
        for i in range(nb)
        for j in range(i + 1)
    ]
    gram_flat = jnp.concatenate(lower_blocks, axis=0).reshape(-1, 128)
    gram_sum = tree_sum(gram_flat, bits, 3).reshape(len(lower_blocks), block, block)
    cross_bits = bits[:1] + bits[7:] + bits[4:7] + bits[1:4]
    cross = tree_sum(cross_part.reshape(-1, 128), cross_bits, 3).reshape(width, attrs)
    block_of = {}
    for n, (i, j) in enumerate((i, j) for i in range(nb) for j in range(i + 1)):
        block_of[(i, j)] = gram_sum[n]
        block_of[(j, i)] = gram_sum[n].T
    gram = jnp.concatenate(
        [jnp.concatenate([block_of[(i, j)] for j in range(nb)], axis=1) for i in range(nb)],
        axis=0,
    )
    total_rows = embeddings.shape[0] * lax.axis_size("docs") * lax.axis_size("grp")
    ridge_shift = penalty[0].astype(jnp.float32) * jnp.float32(total_rows / 8.0)
    system = gram + ridge_shift * jnp.eye(width, dtype=jnp.float32)
    factor, inverses = blocked_cholesky(system, block)
    coeffs = cholesky_solve(factor, inverses, cross, block).astype(jnp.bfloat16)
    scores = jnp.dot(features, coeffs, preferred_element_type=jnp.float32)
    peak_local = jnp.max(jnp.abs(scores), axis=0)
    column_sum = jnp.sum(scores, axis=0)
    stats = peak_and_total(jnp.stack([peak_local, column_sum]), bits)
    peak = stats[0]
    total = stats[1]
    quality = (scores - total / jnp.float32(total_rows)) / (peak + 1e-06)
    return quality.astype(jnp.bfloat16)


def solution(mesh):
    in_specs = (
        P(("docs", "grp"), None),
        P(),
        P(),
        P(),
        P(("docs", "grp"), None),
        P(("docs", "grp"), None),
    )
    out_specs = P(("docs", "grp"), None)
    return jax.shard_map(
        on_device, mesh=mesh, in_specs=in_specs, out_specs=out_specs, check_vma=False
    )
```

```python
import math

import jax
import jax.numpy as jnp
from jax import lax
from jax.sharding import PartitionSpec as P


def phase_table(phase_code, width):
    feature_ids = jnp.arange(width, dtype=jnp.int32)
    code_value = phase_code[0]
    index_value = (code_value * 389 + feature_ids * (feature_ids + code_value) * 53) % 4096
    return index_value.astype(jnp.float32) * (2.0 * math.pi / 4096.0)


def exchange_bits(axis_sizes):
    bits = []
    for name, size in axis_sizes:
        mask = 1
        while mask < size:
            bits.append((name, size, mask))
            mask *= 2
    return bits


def partner(x, name, size, mask):
    return lax.ppermute(x, name, [(i, i ^ mask) for i in range(size)])


def tree_sum(x, bits, halving):
    for name, size, mask in bits[:halving]:
        half = x.shape[0] // 2
        bit = (lax.axis_index(name) // mask) % 2
        keep = lax.dynamic_slice_in_dim(x, bit * half, half, 0)
        send = lax.dynamic_slice_in_dim(x, (1 - bit) * half, half, 0)
        x = keep + partner(send, name, size, mask)
    for name, size, mask in bits[halving:]:
        x = x + partner(x, name, size, mask)
    for name, size, mask in reversed(bits[:halving]):
        bit = (lax.axis_index(name) // mask) % 2
        other = partner(x, name, size, mask)
        x = jnp.where(bit == 0, jnp.concatenate([x, other]), jnp.concatenate([other, x]))
    return x


def peak_and_total(stats, bits):
    for name, size, mask in bits:
        other = partner(stats, name, size, mask)
        stats = jnp.concatenate(
            [jnp.maximum(stats[:1], other[:1]), stats[1:] + other[1:]], axis=0
        )
    return stats


HIGHEST = lax.Precision.HIGHEST


def triangular_inverse(lower):
    size = lower.shape[0]
    eye = jnp.eye(size, dtype=lower.dtype)
    pivots = jnp.sum(lower * eye, axis=1)
    power = eye - lower / pivots[:, None]
    product = eye + power
    reach = 2
    while reach < size:
        power = jnp.dot(power, power, precision=HIGHEST)
        product = jnp.dot(product, eye + power, precision=HIGHEST)
        reach *= 2
    return product / pivots[None, :]


def blocked_cholesky(system, block):
    count = system.shape[0] // block
    trailing = system
    columns = []
    inverses = []
    for k in range(count):
        head = lax.linalg.cholesky(trailing[:block, :block], symmetrize_input=False)
        inverse = triangular_inverse(head)
        inverses.append(inverse)
        above = [jnp.zeros((k * block, block), system.dtype)] if k else []
        if k < count - 1:
            panel = jnp.dot(trailing[block:, :block], inverse.T, precision=HIGHEST)
            trailing = trailing[block:, block:] - jnp.dot(panel, panel.T, precision=HIGHEST)
            columns.append(jnp.concatenate(above + [head, panel]))
        else:
            columns.append(jnp.concatenate(above + [head]))
    return jnp.concatenate(columns, axis=1), inverses


def cholesky_solve(factor, inverses, rhs, block):
    count = factor.shape[0] // block
    forward = []
    for k in range(count):
        rows = slice(k * block, (k + 1) * block)
        residual = rhs[rows]
        if k:
            residual = residual - jnp.dot(
                factor[rows, :k * block], jnp.concatenate(forward), precision=HIGHEST
            )
        forward.append(jnp.dot(inverses[k], residual, precision=HIGHEST))
    backward = [None] * count
    for k in reversed(range(count)):
        residual = forward[k]
        if k < count - 1:
            below = factor[(k + 1) * block:, k * block:(k + 1) * block]
            residual = residual - jnp.dot(
                below.T, jnp.concatenate(backward[k + 1:]), precision=HIGHEST
            )
        backward[k] = jnp.dot(inverses[k].T, residual, precision=HIGHEST)
    return jnp.concatenate(backward)


def on_device(embeddings, projection, phase_code, penalty, assignment, targets):
    width = projection.shape[1]
    attrs = targets.shape[1]
    bits = exchange_bits([("docs", lax.axis_size("docs")), ("grp", lax.axis_size("grp"))])
    phases = phase_table(phase_code, width)
    projected = jnp.dot(embeddings, projection, preferred_element_type=jnp.float32)
    features = jnp.cos(projected + phases).astype(jnp.bfloat16)
    aligned = features[assignment.reshape(-1)]
    gram_part = lax.dot_general(
        features, features, (((0,), (0,)), ((), ())), preferred_element_type=jnp.float32
    )
    cross_part = lax.dot_general(
        aligned, targets, (((0,), (0,)), ((), ())), preferred_element_type=jnp.float32
    )
    block = 128
    nb = width // block
    lower_blocks = [
        gram_part[i * block:(i + 1) * block, j * block:(j + 1) * block]
        for i in range(nb)
        for j in range(i + 1)
    ]
    gram_flat = jnp.concatenate(lower_blocks, axis=0).reshape(-1, 128)
    gram_sum = tree_sum(gram_flat, bits, 3).reshape(len(lower_blocks), block, block)
    cross_bits = bits[:1] + bits[4:7] + bits[1:4] + bits[7:]
    cross = tree_sum(cross_part.reshape(-1, 128), cross_bits, 3).reshape(width, attrs)
    block_of = {}
    for n, (i, j) in enumerate((i, j) for i in range(nb) for j in range(i + 1)):
        block_of[(i, j)] = gram_sum[n]
        if j < i:
            block_of[(j, i)] = jnp.zeros_like(gram_sum[n])
    gram = jnp.concatenate(
        [jnp.concatenate([block_of[(i, j)] for j in range(nb)], axis=1) for i in range(nb)],
        axis=0,
    )
    total_rows = embeddings.shape[0] * lax.axis_size("docs") * lax.axis_size("grp")
    ridge_shift = penalty[0].astype(jnp.float32) * jnp.float32(total_rows / 8.0)
    system = gram + ridge_shift * jnp.eye(width, dtype=jnp.float32)
    factor, inverses = blocked_cholesky(system, block)
    coeffs = cholesky_solve(factor, inverses, cross, block).astype(jnp.bfloat16)
    scores = jnp.dot(features, coeffs, preferred_element_type=jnp.float32)
    peak_local = jnp.max(jnp.abs(scores), axis=0)
    column_sum = jnp.sum(scores, axis=0)
    stats = peak_and_total(jnp.stack([peak_local, column_sum]), bits)
    peak = stats[0]
    total = stats[1]
    quality = (scores - total / jnp.float32(total_rows)) / (peak + 1e-06)
    return quality.astype(jnp.bfloat16)


def solution(mesh):
    in_specs = (
        P(("docs", "grp"), None),
        P(),
        P(),
        P(),
        P(("docs", "grp"), None),
        P(("docs", "grp"), None),
    )
    out_specs = P(("docs", "grp"), None)
    return jax.shard_map(
        on_device, mesh=mesh, in_specs=in_specs, out_specs=out_specs, check_vma=False
    )
```

```python
import math

import jax
import jax.numpy as jnp
from jax import lax
from jax.sharding import PartitionSpec as P


def phase_table(phase_code, width):
    feature_ids = jnp.arange(width, dtype=jnp.int32)
    code_value = phase_code[0]
    index_value = (code_value * 389 + feature_ids * (feature_ids + code_value) * 53) % 4096
    return index_value.astype(jnp.float32) * (2.0 * math.pi / 4096.0)


def exchange_bits(axis_sizes):
    bits = []
    for name, size in axis_sizes:
        mask = 1
        while mask < size:
            bits.append((name, size, mask))
            mask *= 2
    return bits


def partner(x, name, size, mask):
    return lax.ppermute(x, name, [(i, i ^ mask) for i in range(size)])


def tree_sum(x, bits, halving):
    for name, size, mask in bits[:halving]:
        half = x.shape[0] // 2
        bit = (lax.axis_index(name) // mask) % 2
        keep = lax.dynamic_slice_in_dim(x, bit * half, half, 0)
        send = lax.dynamic_slice_in_dim(x, (1 - bit) * half, half, 0)
        x = keep + partner(send, name, size, mask)
    for name, size, mask in bits[halving:]:
        x = x + partner(x, name, size, mask)
    for name, size, mask in reversed(bits[:halving]):
        bit = (lax.axis_index(name) // mask) % 2
        other = partner(x, name, size, mask)
        x = jnp.where(bit == 0, jnp.concatenate([x, other]), jnp.concatenate([other, x]))
    return x


def peak_and_total(stats, bits):
    for name, size, mask in bits:
        other = partner(stats, name, size, mask)
        stats = jnp.concatenate(
            [jnp.maximum(stats[:1], other[:1]), stats[1:] + other[1:]], axis=0
        )
    return stats


HIGHEST = lax.Precision.HIGHEST


def triangular_inverse(lower):
    size = lower.shape[0]
    eye = jnp.eye(size, dtype=lower.dtype)
    pivots = jnp.sum(lower * eye, axis=1)
    power = eye - lower / pivots[:, None]
    product = eye + power
    reach = 2
    while reach < size:
        power = jnp.dot(power, power, precision=HIGHEST)
        product = jnp.dot(product, eye + power, precision=HIGHEST)
        reach *= 2
    return product / pivots[None, :]


def blocked_cholesky(system, block):
    count = system.shape[0] // block
    trailing = system
    columns = []
    inverses = []
    for k in range(count):
        head = lax.linalg.cholesky(trailing[:block, :block], symmetrize_input=False)
        inverse = triangular_inverse(head)
        inverses.append(inverse)
        above = [jnp.zeros((k * block, block), system.dtype)] if k else []
        if k < count - 1:
            panel = jnp.dot(trailing[block:, :block], inverse.T, precision=HIGHEST)
            trailing = trailing[block:, block:] - jnp.dot(panel, panel.T, precision=HIGHEST)
            columns.append(jnp.concatenate(above + [head, panel]))
        else:
            columns.append(jnp.concatenate(above + [head]))
    return jnp.concatenate(columns, axis=1), inverses


def cholesky_solve(factor, inverses, rhs, block):
    count = factor.shape[0] // block
    forward = []
    for k in range(count):
        rows = slice(k * block, (k + 1) * block)
        residual = rhs[rows]
        if k:
            residual = residual - jnp.dot(
                factor[rows, :k * block], jnp.concatenate(forward), precision=HIGHEST
            )
        forward.append(jnp.dot(inverses[k], residual, precision=HIGHEST))
    backward = [None] * count
    for k in reversed(range(count)):
        residual = forward[k]
        if k < count - 1:
            below = factor[(k + 1) * block:, k * block:(k + 1) * block]
            residual = residual - jnp.dot(
                below.T, jnp.concatenate(backward[k + 1:]), precision=HIGHEST
            )
        backward[k] = jnp.dot(inverses[k].T, residual, precision=HIGHEST)
    return jnp.concatenate(backward)


def on_device(embeddings, projection, phase_code, penalty, assignment, targets):
    width = projection.shape[1]
    attrs = targets.shape[1]
    bits = exchange_bits([("docs", lax.axis_size("docs")), ("grp", lax.axis_size("grp"))])
    phases = phase_table(phase_code, width)
    projected = jnp.dot(embeddings, projection, preferred_element_type=jnp.float32)
    features = jnp.cos(projected + phases).astype(jnp.bfloat16)
    aligned = features[assignment.reshape(-1)]
    gram_part = lax.dot_general(
        features, features, (((0,), (0,)), ((), ())), preferred_element_type=jnp.float32
    )
    cross_part = lax.dot_general(
        aligned, targets, (((0,), (0,)), ((), ())), preferred_element_type=jnp.float32
    )
    block = 128
    nb = width // block
    lower_blocks = [
        gram_part[i * block:(i + 1) * block, j * block:(j + 1) * block]
        for i in range(nb)
        for j in range(i + 1)
    ]
    gram_flat = jnp.concatenate(lower_blocks, axis=0).reshape(-1, 128)
    gram_sum = tree_sum(gram_flat, bits, 4).reshape(len(lower_blocks), block, block)
    cross_bits = bits[:1] + bits[4:7] + bits[1:4] + bits[7:]
    cross = tree_sum(cross_part.reshape(-1, 128), cross_bits, 4).reshape(width, attrs)
    block_of = {}
    for n, (i, j) in enumerate((i, j) for i in range(nb) for j in range(i + 1)):
        block_of[(i, j)] = gram_sum[n]
        if j < i:
            block_of[(j, i)] = jnp.zeros_like(gram_sum[n])
    gram = jnp.concatenate(
        [jnp.concatenate([block_of[(i, j)] for j in range(nb)], axis=1) for i in range(nb)],
        axis=0,
    )
    total_rows = embeddings.shape[0] * lax.axis_size("docs") * lax.axis_size("grp")
    ridge_shift = penalty[0].astype(jnp.float32) * jnp.float32(total_rows / 8.0)
    system = gram + ridge_shift * jnp.eye(width, dtype=jnp.float32)
    factor, inverses = blocked_cholesky(system, block)
    coeffs = cholesky_solve(factor, inverses, cross, block).astype(jnp.bfloat16)
    scores = jnp.dot(features, coeffs, preferred_element_type=jnp.float32)
    peak_local = jnp.max(jnp.abs(scores), axis=0)
    column_sum = jnp.sum(scores, axis=0)
    stats = peak_and_total(jnp.stack([peak_local, column_sum]), bits)
    peak = stats[0]
    total = stats[1]
    quality = (scores - total / jnp.float32(total_rows)) / (peak + 1e-06)
    return quality.astype(jnp.bfloat16)


def solution(mesh):
    in_specs = (
        P(("docs", "grp"), None),
        P(),
        P(),
        P(),
        P(("docs", "grp"), None),
        P(("docs", "grp"), None),
    )
    out_specs = P(("docs", "grp"), None)
    return jax.shard_map(
        on_device, mesh=mesh, in_specs=in_specs, out_specs=out_specs, check_vma=False
    )
```

```python
import math

import jax
import jax.numpy as jnp
from jax import lax
from jax.sharding import PartitionSpec as P


def phase_table(phase_code, width):
    feature_ids = jnp.arange(width, dtype=jnp.int32)
    code_value = phase_code[0]
    index_value = (code_value * 389 + feature_ids * (feature_ids + code_value) * 53) % 4096
    return index_value.astype(jnp.float32) * (2.0 * math.pi / 4096.0)


def exchange_bits(axis_sizes):
    bits = []
    for name, size in axis_sizes:
        mask = 1
        while mask < size:
            bits.append((name, size, mask))
            mask *= 2
    return bits


def partner(x, name, size, mask):
    return lax.ppermute(x, name, [(i, i ^ mask) for i in range(size)])


def tree_sum(x, bits, halving):
    for name, size, mask in bits[:halving]:
        half = x.shape[0] // 2
        bit = (lax.axis_index(name) // mask) % 2
        keep = lax.dynamic_slice_in_dim(x, bit * half, half, 0)
        send = lax.dynamic_slice_in_dim(x, (1 - bit) * half, half, 0)
        x = keep + partner(send, name, size, mask)
    for name, size, mask in bits[halving:]:
        x = x + partner(x, name, size, mask)
    for name, size, mask in reversed(bits[:halving]):
        bit = (lax.axis_index(name) // mask) % 2
        other = partner(x, name, size, mask)
        x = jnp.where(bit == 0, jnp.concatenate([x, other]), jnp.concatenate([other, x]))
    return x


def peak_and_total(stats, bits):
    for name, size, mask in bits:
        other = partner(stats, name, size, mask)
        stats = jnp.concatenate(
            [jnp.maximum(stats[:1], other[:1]), stats[1:] + other[1:]], axis=0
        )
    return stats


HIGHEST = lax.Precision.HIGHEST


def triangular_inverse(lower):
    size = lower.shape[0]
    eye = jnp.eye(size, dtype=lower.dtype)
    pivots = jnp.sum(lower * eye, axis=1)
    power = eye - lower / pivots[:, None]
    product = eye + power
    reach = 2
    while reach < size:
        power = jnp.dot(power, power, precision=HIGHEST)
        product = jnp.dot(product, eye + power, precision=HIGHEST)
        reach *= 2
    return product / pivots[None, :]


def blocked_cholesky(system, block, first_head, first_column):
    count = system.shape[0] // block
    trailing = system
    columns = []
    inverses = []
    for k in range(count):
        corner = first_head if k == 0 else trailing[:block, :block]
        head = lax.linalg.cholesky(corner, symmetrize_input=False)
        inverse = triangular_inverse(head)
        inverses.append(inverse)
        above = [jnp.zeros((k * block, block), system.dtype)] if k else []
        if k < count - 1:
            below = first_column if k == 0 else trailing[block:, :block]
            panel = jnp.dot(below, inverse.T, precision=HIGHEST)
            trailing = trailing[block:, block:] - jnp.dot(panel, panel.T, precision=HIGHEST)
            columns.append(jnp.concatenate(above + [head, panel]))
        else:
            columns.append(jnp.concatenate(above + [head]))
    return jnp.concatenate(columns, axis=1), inverses


def cholesky_solve(factor, inverses, rhs, block):
    count = factor.shape[0] // block
    forward = []
    for k in range(count):
        rows = slice(k * block, (k + 1) * block)
        residual = rhs[rows]
        if k:
            residual = residual - jnp.dot(
                factor[rows, :k * block], jnp.concatenate(forward), precision=HIGHEST
            )
        forward.append(jnp.dot(inverses[k], residual, precision=HIGHEST))
    backward = [None] * count
    for k in reversed(range(count)):
        residual = forward[k]
        if k < count - 1:
            below = factor[(k + 1) * block:, k * block:(k + 1) * block]
            residual = residual - jnp.dot(
                below.T, jnp.concatenate(backward[k + 1:]), precision=HIGHEST
            )
        backward[k] = jnp.dot(inverses[k].T, residual, precision=HIGHEST)
    return jnp.concatenate(backward)


def on_device(embeddings, projection, phase_code, penalty, assignment, targets):
    width = projection.shape[1]
    attrs = targets.shape[1]
    bits = exchange_bits([("docs", lax.axis_size("docs")), ("grp", lax.axis_size("grp"))])
    phases = phase_table(phase_code, width)
    projected = jnp.dot(embeddings, projection, preferred_element_type=jnp.float32)
    features = jnp.cos(projected + phases).astype(jnp.bfloat16)
    aligned = features[assignment.reshape(-1)]
    gram_part = lax.dot_general(
        features, features, (((0,), (0,)), ((), ())), preferred_element_type=jnp.float32
    )
    cross_part = lax.dot_general(
        aligned, targets, (((0,), (0,)), ((), ())), preferred_element_type=jnp.float32
    )
    block = 128
    nb = width // block
    lower_blocks = [
        gram_part[i * block:(i + 1) * block, j * block:(j + 1) * block]
        for i in range(nb)
        for j in range(i + 1)
    ]
    gram_flat = jnp.concatenate(lower_blocks, axis=0).reshape(-1, 128)
    gram_sum = tree_sum(gram_flat, bits, 3).reshape(len(lower_blocks), block, block)
    cross_bits = bits[:1] + bits[4:7] + bits[1:4] + bits[7:]
    cross = tree_sum(cross_part.reshape(-1, 128), cross_bits, 3).reshape(width, attrs)
    block_of = {}
    for n, (i, j) in enumerate((i, j) for i in range(nb) for j in range(i + 1)):
        block_of[(i, j)] = gram_sum[n]
        if j < i:
            block_of[(j, i)] = jnp.zeros_like(gram_sum[n])
    gram = jnp.concatenate(
        [jnp.concatenate([block_of[(i, j)] for j in range(nb)], axis=1) for i in range(nb)],
        axis=0,
    )
    total_rows = embeddings.shape[0] * lax.axis_size("docs") * lax.axis_size("grp")
    ridge_shift = penalty[0].astype(jnp.float32) * jnp.float32(total_rows / 8.0)
    system = gram + ridge_shift * jnp.eye(width, dtype=jnp.float32)
    first_head = gram_sum[0] + ridge_shift * jnp.eye(block, dtype=jnp.float32)
    first_column = jnp.concatenate([block_of[(i, 0)] for i in range(1, nb)], axis=0)
    factor, inverses = blocked_cholesky(system, block, first_head, first_column)
    coeffs = cholesky_solve(factor, inverses, cross, block).astype(jnp.bfloat16)
    scores = jnp.dot(features, coeffs, preferred_element_type=jnp.float32)
    peak_local = jnp.max(jnp.abs(scores), axis=0)
    column_sum = jnp.sum(scores, axis=0)
    stats = peak_and_total(jnp.stack([peak_local, column_sum]), bits)
    peak = stats[0]
    total = stats[1]
    quality = (scores - total / jnp.float32(total_rows)) / (peak + 1e-06)
    return quality.astype(jnp.bfloat16)


def solution(mesh):
    in_specs = (
        P(("docs", "grp"), None),
        P(),
        P(),
        P(),
        P(("docs", "grp"), None),
        P(("docs", "grp"), None),
    )
    out_specs = P(("docs", "grp"), None)
    return jax.shard_map(
        on_device, mesh=mesh, in_specs=in_specs, out_specs=out_specs, check_vma=False
    )
```
